512 devices in a mesh: fsdp: 128 (over y, z, core), tensor: 4 (over x).
Axes of the slice: x: 4, y: 8, z: 8, core: 2. Of those that a mesh axis runs over, the one named last changes fastest.
Arguments:
- layer_inputs: bfloat16 [2, 49152, 5120], P(None, 'fsdp', 'tensor'), may hold values from -8 to 8, as said below
- out_grads: bfloat16 [2, 49152, 2560], P(None, 'fsdp', 'tensor'), may hold values from -8 to 8, as said below
- weight_grad: bfloat16 [2, 2560, 5120], P(None, 'fsdp', 'tensor'), may hold values from -0.059814453 to 0.059814453
- emb_grad: bfloat16 [50176, 2560], P('fsdp', 'tensor'), may hold values from -0.59765625 to 0.59765625
- counts: int32 [50176], P('fsdp'), may hold values from 0 to 250
- owner_pos: int32 [4, 30], P('tensor'), may hold values from 0 to 127, as said below
Outputs:
- update: bfloat16 [2, 2560, 5120], P(None, 'fsdp', 'tensor')
- owner_inverses: float32 [4, 128, 128, 128], P('tensor', 'fsdp')
- emb_update: bfloat16 [50176, 2560], P('fsdp', 'tensor')
The draws below stay inside these ranges and needn't reach their ends.
Inputs may be any that keep to these rules, and one draw needn't show every extreme that they name: `layer_inputs`: every element lies within the stated range; inner units in groups of four share a common part. `out_grads`: every element lies within the stated range; features in groups of four share a common part. `owner_pos`: the 30 entries of a row are distinct; slot p belongs to fsdp index p; some fsdp index holds 1 block of each row.
All inputs are finite; a program needn't handle non-finite values. Where the reference program divides by a largest or mean magnitude, that divisor is 1e-20 or more.
Results may differ from the reference program's by a relative error of at most 0.0062.
Values may be sent and summed in bfloat16 or wider, within the bound.
No kernel may reach another device: no remote copies, remote signals or barrier semaphores. Data moves between devices by JAX's collectives and lax.ppermute only.
A program may use at most 64 MiB of HBM per device.

```python
import jax
import jax.numpy as jnp
from jax import lax

D = 2560
INNER = 5120
BLK = 128
NS_ITERS = 8
L = 2
ROWS = 49152
VOCAB = 50176
ABLK = 10
GBLK = 5
NBT = 30
POSITIONS = 128
N_TENSOR = 4


def mixed_draw(key, lead_rows, width_all):
    key_base = jax.random.fold_in(key, 11)
    key_own, key_group, key_shift = jax.random.split(key_base, 3)
    own_part = jax.random.truncated_normal(key_own, -4.0, 4.0, (lead_rows, width_all), jnp.float32)
    group_part = jax.random.truncated_normal(key_group, -4.0, 4.0, (lead_rows, width_all // 4), jnp.float32)
    shift_part = jax.random.truncated_normal(key_shift, -4.0, 4.0, (lead_rows, width_all // 4 + 1), jnp.float32)
    group_full = jnp.repeat(group_part, 4, axis=1)
    shift_full = jnp.repeat(shift_part, 4, axis=1)[:, 2:2 + width_all]
    return 0.25 * own_part + group_full + 0.6 * shift_full


def draw_layer_inputs(key, part):
    return mixed_draw(key, L * ROWS, INNER).reshape(L, ROWS, INNER).astype(jnp.bfloat16)


def draw_out_grads(key, part):
    return mixed_draw(jax.random.fold_in(key, 23), L * ROWS, D).reshape(L, ROWS, D).astype(jnp.bfloat16)


def draw_counts(key, part):
    position = jnp.arange(VOCAB, dtype=jnp.int32)
    level = jax.random.randint(jax.random.fold_in(key, 9), (), 1, 9, dtype=jnp.int32)
    ceiling = level * (10 + 20 * position // VOCAB)
    drawn = jax.random.randint(jax.random.fold_in(key, 5), (VOCAB,), 0, ceiling, dtype=jnp.int32)
    return drawn.at[VOCAB - 1].set(250).astype(jnp.int32)


def draw_owner_pos(key, part):

    def one_row(row_key):
        key_pick, key_order = jax.random.split(row_key)
        picked = jax.random.permutation(key_pick, POSITIONS - 1)[:NBT - 1].astype(jnp.int32)
        chosen = jnp.concatenate([picked, jnp.full((1,), POSITIONS - 1, jnp.int32)])
        return jax.random.permutation(key_order, chosen)
    row_keys = jax.random.split(jax.random.fold_in(key, 7), N_TENSOR)
    return jax.vmap(one_row)(row_keys).astype(jnp.int32)


def block_scale(rng, dims, shards, least, largest):
    def one(dim, blocks):
        steps = jax.random.uniform(jax.random.fold_in(jax.random.fold_in(rng, 6), dim), (blocks,), jnp.float32, least / len(shards), largest / len(shards))
        return jnp.repeat(jnp.exp(steps), dims[dim] // blocks).reshape((-1,) + (1,) * (len(dims) - dim - 1))

    loudness = one(*shards[0])
    for cut in shards[1:]:
        loudness = loudness * one(*cut)
    return loudness


def noise(key, dims, scale, limit, pieces=(), kind=jnp.bfloat16):
    entries = jax.random.normal(key, dims, jnp.float32) * scale
    if len(pieces) > 0:
        entries = block_scale(key, dims, pieces, -0.22, 0.18) * entries
    return jnp.clip(entries, min=-limit, max=limit).astype(kind)


def setup_inputs(seed: int = 0) -> dict:
    seeds = jax.random.split(jax.random.key(seed), 7)
    return {
        "layer_inputs": draw_layer_inputs(jax.random.fold_in(seeds[6], 71), 0),
        "out_grads": draw_out_grads(jax.random.fold_in(seeds[6], 71), 0),
        "weight_grad": noise(seeds[2], (L, D, INNER), 0.01, 0.059814453, ((1, 128), (2, 4))),
        "emb_grad": noise(seeds[3], (VOCAB, D), 0.1, 0.59765625, ((0, 128), (1, 4))),
        "counts": draw_counts(jax.random.fold_in(seeds[6], 71), 0),
        "owner_pos": draw_owner_pos(jax.random.fold_in(seeds[6], 71), 0),
    }


DAMP = 0.02
EDAMP = 0.25


def newton_inverse(factor):
    identity = jnp.eye(factor.shape[-1], dtype=jnp.float32)
    damped = factor + DAMP * identity
    norm_scale = jnp.max(jnp.sum(jnp.abs(damped), axis=-1), axis=-1)
    approx = identity[None] / norm_scale[:, None, None]
    for sweep_idx in range(NS_ITERS):
        product = jnp.einsum("bij,bjk->bik", damped, approx, precision=lax.Precision.HIGHEST)
        approx = jnp.einsum("bij,bjk->bik", approx, 2.0 * identity[None] - product, precision=lax.Precision.HIGHEST)
    return approx


def block_factors(data_rows, width_all):
    row_count = data_rows.shape[0]
    blocks = data_rows.reshape(row_count, width_all // BLK, BLK).astype(jnp.float32)
    return jnp.einsum("rbi,rbj->bij", blocks, blocks, precision=lax.Precision.HIGHEST) / row_count


def reference(layer_inputs, out_grads, weight_grad, emb_grad, counts, owner_pos):
    a_list = []
    g_list = []
    for layer_idx in range(L):
        a_list.append(block_factors(layer_inputs[layer_idx], INNER))
        g_list.append(block_factors(out_grads[layer_idx], D))
    a_fac = jnp.stack(a_list)
    g_fac = jnp.stack(g_list)
    a_inv = newton_inverse(a_fac.reshape(-1, BLK, BLK)).reshape(a_fac.shape)
    g_inv = newton_inverse(g_fac.reshape(-1, BLK, BLK)).reshape(g_fac.shape)
    a_split = a_inv.reshape(L, N_TENSOR, ABLK, BLK, BLK)
    g_split = g_inv.reshape(L, N_TENSOR, GBLK, BLK, BLK)
    per_tensor = jnp.concatenate([a_split, g_split], axis=2).transpose(1, 0, 2, 3, 4).reshape(N_TENSOR, NBT, BLK, BLK)
    owner_inverses = jnp.zeros((N_TENSOR, POSITIONS, BLK, BLK), jnp.float32)
    owner_inverses = owner_inverses.at[jnp.arange(N_TENSOR, dtype=jnp.int32)[:, None], owner_pos].set(per_tensor)
    a_low = a_inv.astype(jnp.bfloat16)
    g_low = g_inv.astype(jnp.bfloat16)
    updates = []
    for layer_idx in range(L):
        grad_blocks = weight_grad[layer_idx].reshape(D, INNER // BLK, BLK).astype(jnp.float32)
        right_done = jnp.einsum("dik,ikj->dij", grad_blocks, a_low[layer_idx].astype(jnp.float32), precision=lax.Precision.HIGHEST)
        right_done = right_done.reshape(D, INNER).astype(jnp.bfloat16)
        row_blocks = right_done.reshape(D // BLK, BLK, INNER).astype(jnp.float32)
        left_done = jnp.einsum("jae,jec->jac", g_low[layer_idx].astype(jnp.float32), row_blocks, precision=lax.Precision.HIGHEST)
        updates.append(left_done.reshape(D, INNER).astype(jnp.bfloat16))
    update = jnp.stack(updates)
    count_total = jnp.sum(counts.astype(jnp.float32))
    frequency = counts.astype(jnp.float32) * VOCAB / count_total
    emb_update = (emb_grad.astype(jnp.float32) / (frequency + EDAMP)[:, None]).astype(jnp.bfloat16)
    return (update, owner_inverses, emb_update)
```

```python
import jax
import jax.numpy as jnp
from jax import lax
from jax.sharding import PartitionSpec as P

BLK = 128
NS_ITERS = 8


DAMP = 0.02
EDAMP = 0.25


def newton_inverse(factor):
    identity = jnp.eye(factor.shape[-1], dtype=jnp.float32)
    damped = factor + DAMP * identity
    norm_scale = jnp.max(jnp.sum(jnp.abs(damped), axis=-1), axis=-1)
    approx = identity[None] / norm_scale[:, None, None]

    def sweep(sweep_idx, approx):
        product = jnp.einsum("bij,bjk->bik", damped, approx, precision=lax.Precision.HIGHEST)
        return jnp.einsum(
            "bij,bjk->bik", approx, 2.0 * identity[None] - product, precision=lax.Precision.HIGHEST
        )

    return lax.fori_loop(0, NS_ITERS, sweep, approx)


def on_device(layer_inputs, out_grads, weight_grad, emb_grad, counts, owner_pos):
    fsdp_size = lax.axis_size("fsdp")
    layers, row_count, inner_local = layer_inputs.shape
    width_local = out_grads.shape[2]
    a_count = inner_local // BLK
    g_count = width_local // BLK
    input_blocks = layer_inputs.reshape(layers, row_count, a_count, BLK)
    a_part = jnp.einsum(
        "lrbi,lrbj->lbij", input_blocks, input_blocks, preferred_element_type=jnp.float32
    )
    grad_blocks = out_grads.reshape(layers, row_count, g_count, BLK)
    g_part = jnp.einsum(
        "lrbi,lrbj->lbij", grad_blocks, grad_blocks, preferred_element_type=jnp.float32
    )
    block_total = layers * (a_count + g_count)
    partials = jnp.concatenate([a_part, g_part], axis=1).reshape(block_total * BLK, BLK)
    count_part = jnp.sum(counts.astype(jnp.float32))
    count_rows = jnp.zeros((8, BLK), jnp.float32).at[0, 0].set(count_part)
    packed = jnp.concatenate([partials, count_rows], axis=0)
    summed = lax.psum(packed, "fsdp")
    count_total = summed[block_total * BLK, 0]
    divisor = row_count * fsdp_size
    factors = (summed[: block_total * BLK] / divisor).reshape(block_total, BLK, BLK)
    inv = newton_inverse(factors)
    own_table = owner_pos[0]
    slot = lax.axis_index("fsdp")
    hit = own_table == slot
    pick = jnp.argmax(hit)
    held = lax.dynamic_index_in_dim(inv, pick, axis=0, keepdims=True)
    owner_out = jnp.where(jnp.any(hit), held, 0.0)[None]
    low_inv = inv.astype(jnp.bfloat16).reshape(layers, a_count + g_count, BLK, BLK)
    a_low = low_inv[:, :a_count]
    g_own = low_inv[:, a_count:]
    g_all = lax.all_gather(g_own, "tensor", axis=1, tiled=True)
    d_local = weight_grad.shape[1]
    grad_split = weight_grad.reshape(layers, d_local, a_count, BLK)
    right_done = jnp.einsum(
        "ldbi,lbij->ldbj", grad_split, a_low, preferred_element_type=jnp.float32
    )
    right_done = right_done.reshape(layers, d_local, inner_local).astype(jnp.bfloat16)
    columns = lax.all_to_all(right_done, "fsdp", split_axis=2, concat_axis=1, tiled=True)
    full_width = columns.shape[1]
    column_blocks = columns.reshape(layers, full_width // BLK, BLK, columns.shape[2])
    left_done = jnp.einsum(
        "lbij,lbjc->lbic", g_all, column_blocks, preferred_element_type=jnp.float32
    )
    left_done = left_done.reshape(columns.shape).astype(jnp.bfloat16)
    update = lax.all_to_all(left_done, "fsdp", split_axis=1, concat_axis=2, tiled=True)
    vocab_total = counts.shape[0] * fsdp_size
    frequency = counts.astype(jnp.float32) * vocab_total / count_total
    emb_update = (emb_grad.astype(jnp.float32) / (frequency + EDAMP)[:, None]).astype(jnp.bfloat16)
    return (update, owner_out, emb_update)


def solution(mesh):
    placed = (
        P(None, "fsdp", "tensor"),
        P(None, "fsdp", "tensor"),
        P(None, "fsdp", "tensor"),
        P("fsdp", "tensor"),
        P("fsdp"),
        P("tensor", None),
    )
    return jax.shard_map(
        on_device,
        mesh=mesh,
        in_specs=placed,
        out_specs=(P(None, "fsdp", "tensor"), P("tensor", "fsdp", None, None), P("fsdp", "tensor")),
        check_vma=False,
    )
```

```python
import jax
import jax.numpy as jnp
from jax import lax
from jax.sharding import PartitionSpec as P

BLK = 128
NS_ITERS = 8


DAMP = 0.02
EDAMP = 0.25


def newton_inverse(factor):
    identity = jnp.eye(factor.shape[-1], dtype=jnp.float32)
    damped = factor + DAMP * identity
    norm_scale = jnp.max(jnp.sum(jnp.abs(damped), axis=-1), axis=-1)
    approx = identity[None] / norm_scale[:, None, None]

    def sweep(sweep_idx, approx):
        product = jnp.einsum("bij,bjk->bik", damped, approx, precision=lax.Precision.HIGHEST)
        return jnp.einsum(
            "bij,bjk->bik", approx, 2.0 * identity[None] - product, precision=lax.Precision.HIGHEST
        )

    return lax.fori_loop(0, NS_ITERS, sweep, approx)


def pack_symmetric(blocks, count_part, fsdp_size):
    half = BLK // 2
    rows = lax.broadcasted_iota(jnp.int32, (half, half), 0)
    cols = lax.broadcasted_iota(jnp.int32, (half, half), 1)
    upper_left = blocks[:, :half, :half]
    lower_right = jnp.flip(blocks[:, half:, half:], (1, 2))
    folded = jnp.where(rows < cols, upper_left, lower_right)
    panel = jnp.concatenate([folded, blocks[:, :half, half:]], axis=2)
    diag = jnp.diagonal(upper_left, axis1=1, axis2=2).reshape(-1, BLK)
    count_row = jnp.zeros((1, BLK), jnp.float32).at[0, 0].set(count_part)
    body = jnp.concatenate([panel.reshape(-1, BLK), diag, count_row], axis=0)
    total = -(-body.shape[0] // fsdp_size) * fsdp_size
    return jnp.concatenate([body, jnp.zeros((total - body.shape[0], BLK), jnp.float32)], axis=0)


def unpack_symmetric(summed, block_total):
    half = BLK // 2
    panel = summed[: block_total * half].reshape(block_total, half, BLK)
    diag_rows = block_total * half // BLK
    diag = summed[block_total * half : block_total * half + diag_rows].reshape(block_total, half)
    count_total = summed[block_total * half + diag_rows, 0]
    rows = lax.broadcasted_iota(jnp.int32, (half, half), 0)
    cols = lax.broadcasted_iota(jnp.int32, (half, half), 1)
    folded = panel[:, :, :half]
    upper_right = panel[:, :, half:]
    folded_t = jnp.swapaxes(folded, 1, 2)
    upper_left = jnp.where(rows < cols, folded, jnp.where(rows > cols, folded_t, diag[:, :, None]))
    turned = jnp.flip(folded, (1, 2))
    lower_right = jnp.where(rows <= cols, turned, jnp.swapaxes(turned, 1, 2))
    top = jnp.concatenate([upper_left, upper_right], axis=2)
    bottom = jnp.concatenate([jnp.swapaxes(upper_right, 1, 2), lower_right], axis=2)
    return jnp.concatenate([top, bottom], axis=1), count_total


def sum_over_fsdp(packed, fsdp_size):
    chunk = packed.shape[0] // fsdp_size
    pieces = lax.all_to_all(packed.reshape(fsdp_size, chunk, BLK), "fsdp", 0, 0, tiled=True)
    mine = jnp.sum(pieces, axis=0)
    spread = jnp.broadcast_to(mine[None], (fsdp_size, chunk, BLK))
    return lax.all_to_all(spread, "fsdp", 0, 0, tiled=True).reshape(packed.shape)


def on_device(layer_inputs, out_grads, weight_grad, emb_grad, counts, owner_pos):
    fsdp_size = lax.axis_size("fsdp")
    layers, row_count, inner_local = layer_inputs.shape
    width_local = out_grads.shape[2]
    a_count = inner_local // BLK
    g_count = width_local // BLK
    input_blocks = layer_inputs.reshape(layers, row_count, a_count, BLK)
    a_part = jnp.einsum(
        "lrbi,lrbj->lbij", input_blocks, input_blocks, preferred_element_type=jnp.float32
    )
    grad_blocks = out_grads.reshape(layers, row_count, g_count, BLK)
    g_part = jnp.einsum(
        "lrbi,lrbj->lbij", grad_blocks, grad_blocks, preferred_element_type=jnp.float32
    )
    block_total = layers * (a_count + g_count)
    partials = jnp.concatenate([a_part, g_part], axis=1).reshape(block_total, BLK, BLK)
    count_part = jnp.sum(counts.astype(jnp.float32))
    packed = pack_symmetric(partials, count_part, fsdp_size)
    summed = sum_over_fsdp(packed, fsdp_size)
    blocks_sum, count_total = unpack_symmetric(summed, block_total)
    divisor = row_count * fsdp_size
    factors = blocks_sum / divisor
    inv = newton_inverse(factors)
    own_table = owner_pos[0]
    slot = lax.axis_index("fsdp")
    hit = own_table == slot
    pick = jnp.argmax(hit)
    held = lax.dynamic_index_in_dim(inv, pick, axis=0, keepdims=True)
    owner_out = jnp.where(jnp.any(hit), held, 0.0)[None]
    low_inv = inv.astype(jnp.bfloat16).reshape(layers, a_count + g_count, BLK, BLK)
    a_low = low_inv[:, :a_count]
    g_own = low_inv[:, a_count:]
    g_all = lax.all_gather(g_own, "tensor", axis=1, tiled=True)
    d_local = weight_grad.shape[1]
    grad_split = weight_grad.reshape(layers, d_local, a_count, BLK)
    right_done = jnp.einsum(
        "ldbi,lbij->ldbj", grad_split, a_low, preferred_element_type=jnp.float32
    )
    right_done = right_done.reshape(layers, d_local, inner_local).astype(jnp.bfloat16)
    columns = lax.all_to_all(right_done, "fsdp", split_axis=2, concat_axis=1, tiled=True)
    full_width = columns.shape[1]
    column_blocks = columns.reshape(layers, full_width // BLK, BLK, columns.shape[2])
    left_done = jnp.einsum(
        "lbij,lbjc->lbic", g_all, column_blocks, preferred_element_type=jnp.float32
    )
    left_done = left_done.reshape(columns.shape).astype(jnp.bfloat16)
    update = lax.all_to_all(left_done, "fsdp", split_axis=1, concat_axis=2, tiled=True)
    vocab_total = counts.shape[0] * fsdp_size
    frequency = counts.astype(jnp.float32) * vocab_total / count_total
    emb_update = (emb_grad.astype(jnp.float32) / (frequency + EDAMP)[:, None]).astype(jnp.bfloat16)
    return (update, owner_out, emb_update)


def solution(mesh):
    placed = (
        P(None, "fsdp", "tensor"),
        P(None, "fsdp", "tensor"),
        P(None, "fsdp", "tensor"),
        P("fsdp", "tensor"),
        P("fsdp"),
        P("tensor", None),
    )
    return jax.shard_map(
        on_device,
        mesh=mesh,
        in_specs=placed,
        out_specs=(P(None, "fsdp", "tensor"), P("tensor", "fsdp", None, None), P("fsdp", "tensor")),
        check_vma=False,
    )
```

```python
import jax
import jax.numpy as jnp
from jax import lax
from jax.sharding import PartitionSpec as P

BLK = 128
NS_ITERS = 8


DAMP = 0.02
EDAMP = 0.25


def newton_inverse(factor):
    identity = jnp.eye(factor.shape[-1], dtype=jnp.float32)
    damped = factor + DAMP * identity
    norm_scale = jnp.max(jnp.sum(jnp.abs(damped), axis=-1), axis=-1)
    approx = identity[None] / norm_scale[:, None, None]

    def sweep(sweep_idx, approx):
        product = jnp.einsum("bij,bjk->bik", damped, approx, precision=lax.Precision.HIGH)
        return jnp.einsum(
            "bij,bjk->bik", approx, 2.0 * identity[None] - product, precision=lax.Precision.HIGH
        )

    return lax.fori_loop(0, NS_ITERS, sweep, approx)


def pack_symmetric(blocks, count_part, fsdp_size):
    half = BLK // 2
    rows = lax.broadcasted_iota(jnp.int32, (half, half), 0)
    cols = lax.broadcasted_iota(jnp.int32, (half, half), 1)
    upper_left = blocks[:, :half, :half]
    lower_right = jnp.swapaxes(blocks[:, half:, half:], 1, 2)
    folded = jnp.where(rows < cols, upper_left, lower_right)
    panel = jnp.concatenate([folded, blocks[:, :half, half:]], axis=2)
    diag = jnp.diagonal(upper_left, axis1=1, axis2=2).reshape(-1, BLK)
    count_row = jnp.zeros((1, BLK), jnp.float32).at[0, 0].set(count_part)
    body = jnp.concatenate([panel.reshape(-1, BLK), diag, count_row], axis=0)
    total = -(-body.shape[0] // fsdp_size) * fsdp_size
    return jnp.concatenate([body, jnp.zeros((total - body.shape[0], BLK), jnp.float32)], axis=0)


def unpack_symmetric(summed, block_total):
    half = BLK // 2
    panel = summed[: block_total * half].reshape(block_total, half, BLK)
    diag_rows = block_total * half // BLK
    diag = summed[block_total * half : block_total * half + diag_rows].reshape(block_total, half)
    count_total = summed[block_total * half + diag_rows, 0]
    rows = lax.broadcasted_iota(jnp.int32, (half, half), 0)
    cols = lax.broadcasted_iota(jnp.int32, (half, half), 1)
    folded = panel[:, :, :half]
    upper_right = panel[:, :, half:]
    folded_t = jnp.swapaxes(folded, 1, 2)
    upper_left = jnp.where(rows < cols, folded, jnp.where(rows > cols, folded_t, diag[:, :, None]))
    lower_right = jnp.where(rows <= cols, folded_t, folded)
    top = jnp.concatenate([upper_left, upper_right], axis=2)
    bottom = jnp.concatenate([jnp.swapaxes(upper_right, 1, 2), lower_right], axis=2)
    return jnp.concatenate([top, bottom], axis=1), count_total


def sum_over_fsdp(packed, fsdp_size):
    chunk = packed.shape[0] // fsdp_size
    pieces = lax.all_to_all(packed.reshape(fsdp_size, chunk, BLK), "fsdp", 0, 0, tiled=True)
    mine = jnp.sum(pieces, axis=0)
    spread = jnp.broadcast_to(mine[None], (fsdp_size, chunk, BLK))
    return lax.all_to_all(spread, "fsdp", 0, 0, tiled=True).reshape(packed.shape)


def on_device(layer_inputs, out_grads, weight_grad, emb_grad, counts, owner_pos):
    fsdp_size = lax.axis_size("fsdp")
    layers, row_count, inner_local = layer_inputs.shape
    width_local = out_grads.shape[2]
    a_count = inner_local // BLK
    g_count = width_local // BLK
    input_blocks = layer_inputs.reshape(layers, row_count, a_count, BLK)
    a_part = jnp.einsum(
        "lrbi,lrbj->lbij", input_blocks, input_blocks, preferred_element_type=jnp.float32
    )
    grad_blocks = out_grads.reshape(layers, row_count, g_count, BLK)
    g_part = jnp.einsum(
        "lrbi,lrbj->lbij", grad_blocks, grad_blocks, preferred_element_type=jnp.float32
    )
    block_total = layers * (a_count + g_count)
    partials = jnp.concatenate([a_part, g_part], axis=1).reshape(block_total, BLK, BLK)
    count_part = jnp.sum(counts.astype(jnp.float32))
    packed = pack_symmetric(partials, count_part, fsdp_size)
    summed = sum_over_fsdp(packed, fsdp_size)
    blocks_sum, count_total = unpack_symmetric(summed, block_total)
    divisor = row_count * fsdp_size
    factors = blocks_sum / divisor
    inv = newton_inverse(factors)
    own_table = owner_pos[0]
    slot = lax.axis_index("fsdp")
    hit = own_table == slot
    pick = jnp.argmax(hit)
    held = lax.dynamic_index_in_dim(inv, pick, axis=0, keepdims=True)
    owner_out = jnp.where(jnp.any(hit), held, 0.0)[None]
    low_inv = inv.astype(jnp.bfloat16).reshape(layers, a_count + g_count, BLK, BLK)
    a_low = low_inv[:, :a_count]
    g_own = low_inv[:, a_count:]
    g_all = lax.all_gather(g_own, "tensor", axis=1, tiled=True)
    d_local = weight_grad.shape[1]
    grad_split = weight_grad.reshape(layers, d_local, a_count, BLK)
    right_done = jnp.einsum(
        "ldbi,lbij->ldbj", grad_split, a_low, preferred_element_type=jnp.float32
    )
    right_done = right_done.reshape(layers, d_local, inner_local).astype(jnp.bfloat16)
    columns = lax.all_to_all(right_done, "fsdp", split_axis=2, concat_axis=1, tiled=True)
    full_width = columns.shape[1]
    column_blocks = columns.reshape(layers, full_width // BLK, BLK, columns.shape[2])
    left_done = jnp.einsum(
        "lbij,lbjc->lbic", g_all, column_blocks, preferred_element_type=jnp.float32
    )
    left_done = left_done.reshape(columns.shape).astype(jnp.bfloat16)
    update = lax.all_to_all(left_done, "fsdp", split_axis=1, concat_axis=2, tiled=True)
    vocab_total = counts.shape[0] * fsdp_size
    frequency = counts.astype(jnp.float32) * vocab_total / count_total
    emb_update = (emb_grad.astype(jnp.float32) / (frequency + EDAMP)[:, None]).astype(jnp.bfloat16)
    return (update, owner_out, emb_update)


def solution(mesh):
    placed = (
        P(None, "fsdp", "tensor"),
        P(None, "fsdp", "tensor"),
        P(None, "fsdp", "tensor"),
        P("fsdp", "tensor"),
        P("fsdp"),
        P("tensor", None),
    )
    return jax.shard_map(
        on_device,
        mesh=mesh,
        in_specs=placed,
        out_specs=(P(None, "fsdp", "tensor"), P("tensor", "fsdp", None, None), P("fsdp", "tensor")),
        check_vma=False,
    )
```

```python
import jax
import jax.numpy as jnp
from jax import lax
from jax.sharding import PartitionSpec as P

BLK = 128
NS_ITERS = 8


DAMP = 0.02
EDAMP = 0.25


def newton_inverse(factor):
    identity = jnp.eye(factor.shape[-1], dtype=jnp.float32)
    damped = factor + DAMP * identity
    norm_scale = jnp.max(jnp.sum(jnp.abs(damped), axis=-1), axis=-1)
    approx = identity[None] / norm_scale[:, None, None]

    def sweep(sweep_idx, approx):
        product = jnp.einsum("bij,bjk->bik", damped, approx, precision=lax.Precision.HIGH)
        return jnp.einsum(
            "bij,bjk->bik", approx, 2.0 * identity[None] - product, precision=lax.Precision.HIGH
        )

    return lax.fori_loop(0, NS_ITERS, sweep, approx)


def pack_symmetric(blocks, count_part, fsdp_size):
    half = BLK // 2
    rows = lax.broadcasted_iota(jnp.int32, (half, BLK), 0)
    lanes = lax.broadcasted_iota(jnp.int32, (half, BLK), 1)
    bottom = blocks[:, half:, :]
    panel = jnp.where(lanes >= rows, blocks[:, :half, :], jnp.roll(bottom, half, axis=2))
    diag = jnp.sum(jnp.where(lanes == rows + half, bottom, 0.0), axis=2).reshape(-1, BLK)
    count_row = jnp.zeros((1, BLK), jnp.float32).at[0, 0].set(count_part)
    body = jnp.concatenate([panel.reshape(-1, BLK), diag, count_row], axis=0)
    total = -(-body.shape[0] // fsdp_size) * fsdp_size
    return jnp.concatenate([body, jnp.zeros((total - body.shape[0], BLK), jnp.float32)], axis=0)


def unpack_symmetric(summed, block_total):
    half = BLK // 2
    panel = summed[: block_total * half].reshape(block_total, half, BLK)
    diag_rows = block_total * half // BLK
    diag = summed[block_total * half : block_total * half + diag_rows].reshape(block_total, half)
    count_total = summed[block_total * half + diag_rows, 0]
    rows = lax.broadcasted_iota(jnp.int32, (half, BLK), 0)
    lanes = lax.broadcasted_iota(jnp.int32, (half, BLK), 1)
    top = jnp.where(lanes >= rows, panel, 0.0)
    turned = jnp.roll(panel, half, axis=2)
    bottom = jnp.where((lanes >= half) & (lanes - half < rows), turned, 0.0)
    bottom = jnp.where(lanes - half == rows, diag[:, :, None], bottom)
    tri = jnp.concatenate([top, bottom], axis=1)
    eye = lax.broadcasted_iota(jnp.int32, (BLK, BLK), 0) == lax.broadcasted_iota(jnp.int32, (BLK, BLK), 1)
    return jnp.where(eye, tri, tri + jnp.swapaxes(tri, 1, 2)), count_total


def sum_over_fsdp(packed, fsdp_size):
    chunk = packed.shape[0] // fsdp_size
    pieces = lax.all_to_all(packed.reshape(fsdp_size, chunk, BLK), "fsdp", 0, 0, tiled=True)
    mine = jnp.sum(pieces, axis=0)
    spread = jnp.broadcast_to(mine[None], (fsdp_size, chunk, BLK))
    return lax.all_to_all(spread, "fsdp", 0, 0, tiled=True).reshape(packed.shape)


def on_device(layer_inputs, out_grads, weight_grad, emb_grad, counts, owner_pos):
    fsdp_size = lax.axis_size("fsdp")
    layers, row_count, inner_local = layer_inputs.shape
    width_local = out_grads.shape[2]
    a_count = inner_local // BLK
    g_count = width_local // BLK
    input_blocks = layer_inputs.reshape(layers, row_count, a_count, BLK)
    a_part = jnp.einsum(
        "lrbi,lrbj->lbij", input_blocks, input_blocks, preferred_element_type=jnp.float32
    )
    grad_blocks = out_grads.reshape(layers, row_count, g_count, BLK)
    g_part = jnp.einsum(
        "lrbi,lrbj->lbij", grad_blocks, grad_blocks, preferred_element_type=jnp.float32
    )
    block_total = layers * (a_count + g_count)
    partials = jnp.concatenate([a_part, g_part], axis=1).reshape(block_total, BLK, BLK)
    count_part = jnp.sum(counts.astype(jnp.float32))
    packed = pack_symmetric(partials, count_part, fsdp_size)
    summed = sum_over_fsdp(packed, fsdp_size)
    blocks_sum, count_total = unpack_symmetric(summed, block_total)
    divisor = row_count * fsdp_size
    factors = blocks_sum / divisor
    inv = newton_inverse(factors)
    own_table = owner_pos[0]
    slot = lax.axis_index("fsdp")
    hit = own_table == slot
    pick = jnp.argmax(hit)
    held = lax.dynamic_index_in_dim(inv, pick, axis=0, keepdims=True)
    owner_out = jnp.where(jnp.any(hit), held, 0.0)[None]
    low_inv = inv.astype(jnp.bfloat16).reshape(layers, a_count + g_count, BLK, BLK)
    a_low = low_inv[:, :a_count]
    g_own = low_inv[:, a_count:]
    g_all = lax.all_gather(g_own, "tensor", axis=1, tiled=True)
    d_local = weight_grad.shape[1]
    grad_split = weight_grad.reshape(layers, d_local, a_count, BLK)
    right_done = jnp.einsum(
        "ldbi,lbij->ldbj", grad_split, a_low, preferred_element_type=jnp.float32
    )
    right_done = right_done.reshape(layers, d_local, inner_local).astype(jnp.bfloat16)
    columns = lax.all_to_all(right_done, "fsdp", split_axis=2, concat_axis=1, tiled=True)
    full_width = columns.shape[1]
    column_blocks = columns.reshape(layers, full_width // BLK, BLK, columns.shape[2])
    left_done = jnp.einsum(
        "lbij,lbjc->lbic", g_all, column_blocks, preferred_element_type=jnp.float32
    )
    left_done = left_done.reshape(columns.shape).astype(jnp.bfloat16)
    update = lax.all_to_all(left_done, "fsdp", split_axis=1, concat_axis=2, tiled=True)
    vocab_total = counts.shape[0] * fsdp_size
    frequency = counts.astype(jnp.float32) * vocab_total / count_total
    emb_update = (emb_grad.astype(jnp.float32) / (frequency + EDAMP)[:, None]).astype(jnp.bfloat16)
    return (update, owner_out, emb_update)


def solution(mesh):
    placed = (
        P(None, "fsdp", "tensor"),
        P(None, "fsdp", "tensor"),
        P(None, "fsdp", "tensor"),
        P("fsdp", "tensor"),
        P("fsdp"),
        P("tensor", None),
    )
    return jax.shard_map(
        on_device,
        mesh=mesh,
        in_specs=placed,
        out_specs=(P(None, "fsdp", "tensor"), P("tensor", "fsdp", None, None), P("fsdp", "tensor")),
        check_vma=False,
    )
```

```python
import jax
import jax.numpy as jnp
from jax import lax
from jax.sharding import PartitionSpec as P

BLK = 128
NS_ITERS = 8


DAMP = 0.02
EDAMP = 0.25


def newton_inverse(factor):
    identity = jnp.eye(factor.shape[-1], dtype=jnp.float32)
    damped = factor + DAMP * identity
    norm_scale = jnp.max(jnp.sum(jnp.abs(damped), axis=-1), axis=-1)
    approx = identity[None] / norm_scale[:, None, None]

    def sweep(sweep_idx, approx):
        product = jnp.einsum("bij,bjk->bik", damped, approx, precision=lax.Precision.HIGH)
        return jnp.einsum(
            "bij,bjk->bik", approx, 2.0 * identity[None] - product, precision=lax.Precision.HIGH
        )

    return lax.fori_loop(0, NS_ITERS, sweep, approx)


def pack_symmetric(blocks, count_part, fsdp_size):
    half = BLK // 2
    rows = lax.broadcasted_iota(jnp.int32, (half, BLK), 0)
    lanes = lax.broadcasted_iota(jnp.int32, (half, BLK), 1)
    bottom = blocks[:, half:, :]
    panel = jnp.where(lanes >= rows, blocks[:, :half, :], jnp.roll(bottom, half, axis=2))
    diag = jnp.sum(jnp.where(lanes == rows + half, bottom, 0.0), axis=2).reshape(-1, BLK)
    count_row = jnp.zeros((1, BLK), jnp.float32).at[0, 0].set(count_part)
    body = jnp.concatenate([panel.reshape(-1, BLK), diag, count_row], axis=0)
    total = -(-body.shape[0] // fsdp_size) * fsdp_size
    return jnp.concatenate([body, jnp.zeros((total - body.shape[0], BLK), jnp.float32)], axis=0)


def unpack_symmetric(summed, block_total):
    half = BLK // 2
    panel = summed[: block_total * half].reshape(block_total, half, BLK)
    diag_rows = block_total * half // BLK
    diag = summed[block_total * half : block_total * half + diag_rows].reshape(block_total, half)
    count_total = summed[block_total * half + diag_rows, 0]
    rows = lax.broadcasted_iota(jnp.int32, (half, BLK), 0)
    lanes = lax.broadcasted_iota(jnp.int32, (half, BLK), 1)
    top = jnp.where(lanes >= rows, panel, 0.0)
    turned = jnp.roll(panel, half, axis=2)
    bottom = jnp.where((lanes >= half) & (lanes - half < rows), turned, 0.0)
    bottom = jnp.where(lanes - half == rows, diag[:, :, None], bottom)
    tri = jnp.concatenate([top, bottom], axis=1)
    eye = lax.broadcasted_iota(jnp.int32, (BLK, BLK), 0) == lax.broadcasted_iota(jnp.int32, (BLK, BLK), 1)
    return jnp.where(eye, tri, tri + jnp.swapaxes(tri, 1, 2)), count_total


def sum_over_fsdp(packed, fsdp_size):
    chunk = packed.shape[0] // fsdp_size
    pieces = lax.all_to_all(packed.reshape(fsdp_size, chunk, BLK), "fsdp", 0, 0, tiled=True)
    mine = jnp.sum(pieces, axis=0)
    spread = jnp.broadcast_to(mine[None], (fsdp_size, chunk, BLK))
    return lax.all_to_all(spread, "fsdp", 0, 0, tiled=True).reshape(packed.shape)


def on_device(layer_inputs, out_grads, weight_grad, emb_grad, counts, owner_pos):
    fsdp_size = lax.axis_size("fsdp")
    layers, row_count, inner_local = layer_inputs.shape
    width_local = out_grads.shape[2]
    a_count = inner_local // BLK
    g_count = width_local // BLK
    input_blocks = layer_inputs.reshape(layers, row_count, a_count, BLK)
    a_part = jnp.einsum(
        "lrbi,lrbj->lbij", input_blocks, input_blocks, preferred_element_type=jnp.float32
    )
    grad_blocks = out_grads.reshape(layers, row_count, g_count, BLK)
    g_part = jnp.einsum(
        "lrbi,lrbj->lbij", grad_blocks, grad_blocks, preferred_element_type=jnp.float32
    )
    block_total = layers * (a_count + g_count)
    partials = jnp.concatenate([a_part, g_part], axis=1).reshape(block_total, BLK, BLK)
    count_part = jnp.sum(counts.astype(jnp.float32))
    packed = pack_symmetric(partials, count_part, fsdp_size)
    summed = sum_over_fsdp(packed, fsdp_size)
    blocks_sum, count_total = unpack_symmetric(summed, block_total)
    divisor = row_count * fsdp_size
    factors = blocks_sum / divisor
    core = lax.axis_index("fsdp") % 2
    share = block_total // 2
    mine = newton_inverse(lax.dynamic_slice_in_dim(factors, core * share, share, axis=0))
    other = lax.ppermute(mine, "fsdp", [(i, i ^ 1) for i in range(fsdp_size)])
    inv = jnp.where(core == 0, jnp.concatenate([mine, other]), jnp.concatenate([other, mine]))
    own_table = owner_pos[0]
    slot = lax.axis_index("fsdp")
    hit = own_table == slot
    pick = jnp.argmax(hit)
    held = lax.dynamic_index_in_dim(inv, pick, axis=0, keepdims=True)
    owner_out = jnp.where(jnp.any(hit), held, 0.0)[None]
    low_inv = inv.astype(jnp.bfloat16).reshape(layers, a_count + g_count, BLK, BLK)
    a_low = low_inv[:, :a_count]
    g_own = low_inv[:, a_count:]
    g_all = lax.all_gather(g_own, "tensor", axis=1, tiled=True)
    d_local = weight_grad.shape[1]
    grad_split = weight_grad.reshape(layers, d_local, a_count, BLK)
    right_done = jnp.einsum(
        "ldbi,lbij->ldbj", grad_split, a_low, preferred_element_type=jnp.float32
    )
    right_done = right_done.reshape(layers, d_local, inner_local).astype(jnp.bfloat16)
    columns = lax.all_to_all(right_done, "fsdp", split_axis=2, concat_axis=1, tiled=True)
    full_width = columns.shape[1]
    column_blocks = columns.reshape(layers, full_width // BLK, BLK, columns.shape[2])
    left_done = jnp.einsum(
        "lbij,lbjc->lbic", g_all, column_blocks, preferred_element_type=jnp.float32
    )
    left_done = left_done.reshape(columns.shape).astype(jnp.bfloat16)
    update = lax.all_to_all(left_done, "fsdp", split_axis=1, concat_axis=2, tiled=True)
    vocab_total = counts.shape[0] * fsdp_size
    frequency = counts.astype(jnp.float32) * vocab_total / count_total
    emb_update = (emb_grad.astype(jnp.float32) / (frequency + EDAMP)[:, None]).astype(jnp.bfloat16)
    return (update, owner_out, emb_update)


def solution(mesh):
    placed = (
        P(None, "fsdp", "tensor"),
        P(None, "fsdp", "tensor"),
        P(None, "fsdp", "tensor"),
        P("fsdp", "tensor"),
        P("fsdp"),
        P("tensor", None),
    )
    return jax.shard_map(
        on_device,
        mesh=mesh,
        in_specs=placed,
        out_specs=(P(None, "fsdp", "tensor"), P("tensor", "fsdp", None, None), P("fsdp", "tensor")),
        check_vma=False,
    )
```

```python
import jax
import jax.numpy as jnp
from jax import lax
import numpy as np
from jax.sharding import Mesh, PartitionSpec as P

BLK = 128
FSDP_SIZE = 128
CHIP_AXES = ("y", "z")
FSDP = ("y", "z", "core")
NS_ITERS = 8


DAMP = 0.02
EDAMP = 0.25


def newton_inverse(factor):
    identity = jnp.eye(factor.shape[-1], dtype=jnp.float32)
    damped = factor + DAMP * identity
    norm_scale = jnp.max(jnp.sum(jnp.abs(damped), axis=-1), axis=-1)
    approx = identity[None] / norm_scale[:, None, None]

    def sweep(sweep_idx, approx):
        product = jnp.einsum("bij,bjk->bik", damped, approx, precision=lax.Precision.HIGH)
        return jnp.einsum(
            "bij,bjk->bik", approx, 2.0 * identity[None] - product, precision=lax.Precision.HIGH
        )

    return lax.fori_loop(0, NS_ITERS, sweep, approx)


def pack_symmetric(blocks, count_part, fsdp_size):
    half = BLK // 2
    rows = lax.broadcasted_iota(jnp.int32, (half, BLK), 0)
    lanes = lax.broadcasted_iota(jnp.int32, (half, BLK), 1)
    bottom = blocks[:, half:, :]
    panel = jnp.where(lanes >= rows, blocks[:, :half, :], jnp.roll(bottom, half, axis=2))
    diag = jnp.sum(jnp.where(lanes == rows + half, bottom, 0.0), axis=2).reshape(-1, BLK)
    count_row = jnp.zeros((1, BLK), jnp.float32).at[0, 0].set(count_part)
    body = jnp.concatenate([panel.reshape(-1, BLK), diag, count_row], axis=0)
    total = -(-body.shape[0] // fsdp_size) * fsdp_size
    return jnp.concatenate([body, jnp.zeros((total - body.shape[0], BLK), jnp.float32)], axis=0)


def unpack_symmetric(summed, block_total):
    half = BLK // 2
    panel = summed[: block_total * half].reshape(block_total, half, BLK)
    diag_rows = block_total * half // BLK
    diag = summed[block_total * half : block_total * half + diag_rows].reshape(block_total, half)
    count_total = summed[block_total * half + diag_rows, 0]
    rows = lax.broadcasted_iota(jnp.int32, (half, BLK), 0)
    lanes = lax.broadcasted_iota(jnp.int32, (half, BLK), 1)
    top = jnp.where(lanes >= rows, panel, 0.0)
    turned = jnp.roll(panel, half, axis=2)
    bottom = jnp.where((lanes >= half) & (lanes - half < rows), turned, 0.0)
    bottom = jnp.where(lanes - half == rows, diag[:, :, None], bottom)
    tri = jnp.concatenate([top, bottom], axis=1)
    eye = lax.broadcasted_iota(jnp.int32, (BLK, BLK), 0) == lax.broadcasted_iota(jnp.int32, (BLK, BLK), 1)
    return jnp.where(eye, tri, tri + jnp.swapaxes(tri, 1, 2)), count_total


def sum_over_fsdp(packed, fsdp_size):
    core = lax.axis_index("core")
    chips = fsdp_size // 2
    halves = packed.reshape(2, packed.shape[0] // 2, BLK)
    send = jnp.where(core == 0, halves[1], halves[0])
    keep = jnp.where(core == 0, halves[0], halves[1])
    part = keep + lax.ppermute(send, "core", [(0, 1), (1, 0)])
    chunk = part.shape[0] // chips
    pieces = lax.all_to_all(part.reshape(chips, chunk, BLK), CHIP_AXES, 0, 0, tiled=True)
    mine = jnp.sum(pieces, axis=0)
    spread = jnp.broadcast_to(mine[None], (chips, chunk, BLK))
    own_half = lax.all_to_all(spread, CHIP_AXES, 0, 0, tiled=True).reshape(part.shape)
    other_half = lax.ppermute(own_half, "core", [(0, 1), (1, 0)])
    return jnp.where(
        core == 0,
        jnp.concatenate([own_half, other_half]),
        jnp.concatenate([other_half, own_half]),
    )


def on_device(layer_inputs, out_grads, weight_grad, emb_grad, counts, owner_pos):
    fsdp_size = FSDP_SIZE
    layers, row_count, inner_local = layer_inputs.shape
    width_local = out_grads.shape[2]
    a_count = inner_local // BLK
    g_count = width_local // BLK
    input_blocks = layer_inputs.reshape(layers, row_count, a_count, BLK)
    a_part = jnp.einsum(
        "lrbi,lrbj->lbij", input_blocks, input_blocks, preferred_element_type=jnp.float32
    )
    grad_blocks = out_grads.reshape(layers, row_count, g_count, BLK)
    g_part = jnp.einsum(
        "lrbi,lrbj->lbij", grad_blocks, grad_blocks, preferred_element_type=jnp.float32
    )
    block_total = layers * (a_count + g_count)
    partials = jnp.concatenate([a_part, g_part], axis=1).reshape(block_total, BLK, BLK)
    count_part = jnp.sum(counts.astype(jnp.float32))
    packed = pack_symmetric(partials, count_part, fsdp_size)
    summed = sum_over_fsdp(packed, fsdp_size)
    blocks_sum, count_total = unpack_symmetric(summed, block_total)
    divisor = row_count * fsdp_size
    factors = blocks_sum / divisor
    core = lax.axis_index(FSDP) % 2
    share = block_total // 2
    mine = newton_inverse(lax.dynamic_slice_in_dim(factors, core * share, share, axis=0))
    other = lax.ppermute(mine, FSDP, [(i, i ^ 1) for i in range(fsdp_size)])
    inv = jnp.where(core == 0, jnp.concatenate([mine, other]), jnp.concatenate([other, mine]))
    own_table = owner_pos[0]
    slot = lax.axis_index(FSDP)
    hit = own_table == slot
    pick = jnp.argmax(hit)
    held = lax.dynamic_index_in_dim(inv, pick, axis=0, keepdims=True)
    owner_out = jnp.where(jnp.any(hit), held, 0.0)[None]
    low_inv = inv.astype(jnp.bfloat16).reshape(layers, a_count + g_count, BLK, BLK)
    a_low = low_inv[:, :a_count]
    g_own = low_inv[:, a_count:]
    g_all = lax.all_gather(g_own, "tensor", axis=1, tiled=True)
    d_local = weight_grad.shape[1]
    grad_split = weight_grad.reshape(layers, d_local, a_count, BLK)
    right_done = jnp.einsum(
        "ldbi,lbij->ldbj", grad_split, a_low, preferred_element_type=jnp.float32
    )
    right_done = right_done.reshape(layers, d_local, inner_local).astype(jnp.bfloat16)
    columns = lax.all_to_all(right_done, FSDP, split_axis=2, concat_axis=1, tiled=True)
    full_width = columns.shape[1]
    column_blocks = columns.reshape(layers, full_width // BLK, BLK, columns.shape[2])
    left_done = jnp.einsum(
        "lbij,lbjc->lbic", g_all, column_blocks, preferred_element_type=jnp.float32
    )
    left_done = left_done.reshape(columns.shape).astype(jnp.bfloat16)
    update = lax.all_to_all(left_done, FSDP, split_axis=1, concat_axis=2, tiled=True)
    vocab_total = counts.shape[0] * fsdp_size
    frequency = counts.astype(jnp.float32) * vocab_total / count_total
    emb_update = (emb_grad.astype(jnp.float32) / (frequency + EDAMP)[:, None]).astype(jnp.bfloat16)
    return (update, owner_out, emb_update)


def solution(mesh):
    fine = Mesh(np.asarray(mesh.devices).reshape(8, 8, 2, -1), FSDP + ("tensor",))
    placed = (
        P(None, FSDP, "tensor"),
        P(None, FSDP, "tensor"),
        P(None, FSDP, "tensor"),
        P(FSDP, "tensor"),
        P(FSDP),
        P("tensor", None),
    )
    return jax.shard_map(
        on_device,
        mesh=fine,
        in_specs=placed,
        out_specs=(P(None, FSDP, "tensor"), P("tensor", FSDP, None, None), P(FSDP, "tensor")),
        check_vma=False,
    )
```

```python
import jax
import jax.numpy as jnp
from jax import lax
import numpy as np
from jax.sharding import Mesh, PartitionSpec as P

BLK = 128
FSDP_SIZE = 128
CHIP_AXES = ("y", "z")
FSDP = ("y", "z", "core")
NS_ITERS = 8


DAMP = 0.02
EDAMP = 0.25


def newton_inverse(factor):
    identity = jnp.eye(factor.shape[-1], dtype=jnp.float32)
    damped = factor + DAMP * identity
    norm_scale = jnp.max(jnp.sum(jnp.abs(damped), axis=-1), axis=-1)
    approx = identity[None] / norm_scale[:, None, None]

    def sweep(sweep_idx, approx):
        product = jnp.einsum("bij,bjk->bik", damped, approx, precision=lax.Precision.HIGH)
        return jnp.einsum(
            "bij,bjk->bik", approx, 2.0 * identity[None] - product, precision=lax.Precision.HIGH
        )

    return lax.fori_loop(0, NS_ITERS, sweep, approx)


def pack_symmetric(blocks, count_part, fsdp_size):
    half = BLK // 2
    rows = lax.broadcasted_iota(jnp.int32, (half, BLK), 0)
    lanes = lax.broadcasted_iota(jnp.int32, (half, BLK), 1)
    bottom = blocks[:, half:, :]
    panel = jnp.where(lanes >= rows, blocks[:, :half, :], jnp.roll(bottom, half, axis=2))
    diag = jnp.sum(jnp.where(lanes == rows + half, bottom, 0.0), axis=2).reshape(-1, BLK)
    count_row = jnp.zeros((1, BLK), jnp.float32).at[0, 0].set(count_part)
    body = jnp.concatenate([panel.reshape(-1, BLK), diag, count_row], axis=0)
    total = -(-body.shape[0] // fsdp_size) * fsdp_size
    return jnp.concatenate([body, jnp.zeros((total - body.shape[0], BLK), jnp.float32)], axis=0)


def unpack_symmetric(summed, block_total):
    half = BLK // 2
    panel = summed[: block_total * half].reshape(block_total, half, BLK)
    diag_rows = block_total * half // BLK
    diag = summed[block_total * half : block_total * half + diag_rows].reshape(block_total, half)
    count_total = summed[block_total * half + diag_rows, 0]
    rows = lax.broadcasted_iota(jnp.int32, (half, BLK), 0)
    lanes = lax.broadcasted_iota(jnp.int32, (half, BLK), 1)
    top = jnp.where(lanes >= rows, panel, 0.0)
    turned = jnp.roll(panel, half, axis=2)
    bottom = jnp.where((lanes >= half) & (lanes - half < rows), turned, 0.0)
    bottom = jnp.where(lanes - half == rows, diag[:, :, None], bottom)
    tri = jnp.concatenate([top, bottom], axis=1)
    eye = lax.broadcasted_iota(jnp.int32, (BLK, BLK), 0) == lax.broadcasted_iota(jnp.int32, (BLK, BLK), 1)
    return jnp.where(eye, tri, tri + jnp.swapaxes(tri, 1, 2)), count_total


def sum_over_fsdp(packed, fsdp_size):
    core = lax.axis_index("core")
    chips = fsdp_size // 2
    halves = packed.reshape(2, packed.shape[0] // 2, BLK)
    send = jnp.where(core == 0, halves[1], halves[0])
    keep = jnp.where(core == 0, halves[0], halves[1])
    part = keep + lax.ppermute(send, "core", [(0, 1), (1, 0)])
    chunk = part.shape[0] // chips
    pieces = lax.all_to_all(part.reshape(chips, chunk, BLK), CHIP_AXES, 0, 0, tiled=True)
    mine = jnp.sum(pieces, axis=0)
    spread = jnp.broadcast_to(mine[None], (chips, chunk, BLK))
    own_half = lax.all_to_all(spread, CHIP_AXES, 0, 0, tiled=True).reshape(part.shape)
    other_half = lax.ppermute(own_half, "core", [(0, 1), (1, 0)])
    return jnp.where(
        core == 0,
        jnp.concatenate([own_half, other_half]),
        jnp.concatenate([other_half, own_half]),
    )


def on_device(layer_inputs, out_grads, weight_grad, emb_grad, counts, owner_pos):
    fsdp_size = FSDP_SIZE
    layers, row_count, inner_local = layer_inputs.shape
    width_local = out_grads.shape[2]
    a_count = inner_local // BLK
    g_count = width_local // BLK
    input_blocks = layer_inputs.reshape(layers, row_count, a_count, BLK)
    a_part = jnp.einsum(
        "lrbi,lrbj->lbij", input_blocks, input_blocks, preferred_element_type=jnp.float32
    )
    grad_blocks = out_grads.reshape(layers, row_count, g_count, BLK)
    g_part = jnp.einsum(
        "lrbi,lrbj->lbij", grad_blocks, grad_blocks, preferred_element_type=jnp.float32
    )
    block_total = layers * (a_count + g_count)
    partials = jnp.concatenate([a_part, g_part], axis=1).reshape(block_total, BLK, BLK)
    count_part = jnp.sum(counts.astype(jnp.float32))
    packed = pack_symmetric(partials, count_part, fsdp_size)
    summed = sum_over_fsdp(packed, fsdp_size)
    blocks_sum, count_total = unpack_symmetric(summed, block_total)
    divisor = row_count * fsdp_size
    factors = blocks_sum / divisor
    core = lax.axis_index(FSDP) % 2
    share = block_total // 2
    mine = newton_inverse(lax.dynamic_slice_in_dim(factors, core * share, share, axis=0))
    other = lax.ppermute(mine, FSDP, [(i, i ^ 1) for i in range(fsdp_size)])
    inv = jnp.where(core == 0, jnp.concatenate([mine, other]), jnp.concatenate([other, mine]))
    own_table = owner_pos[0]
    slot = lax.axis_index(FSDP)
    hit = own_table == slot
    pick = jnp.argmax(hit)
    held = lax.dynamic_index_in_dim(inv, pick, axis=0, keepdims=True)
    owner_out = jnp.where(jnp.any(hit), held, 0.0)[None]
    low_inv = inv.astype(jnp.bfloat16).reshape(layers, a_count + g_count, BLK, BLK)
    a_low = low_inv[:, :a_count]
    g_own = low_inv[:, a_count:]
    g_all = lax.all_gather(g_own, "tensor", axis=1, tiled=True)
    d_local = weight_grad.shape[1]
    grad_split = weight_grad.reshape(layers, d_local, a_count, BLK)
    right_done = jnp.einsum(
        "ldbi,lbij->ldbj", grad_split, a_low, preferred_element_type=jnp.float32
    )
    right_done = right_done.reshape(layers, d_local, inner_local).astype(jnp.bfloat16)
    chips = fsdp_size // 2
    by_chip = lax.all_to_all(right_done, CHIP_AXES, split_axis=2, concat_axis=1, tiled=True)
    by_core = lax.all_to_all(by_chip, "core", split_axis=2, concat_axis=1, tiled=True)
    col_count = by_core.shape[2]
    columns = jnp.swapaxes(by_core.reshape(layers, 2, chips, d_local, col_count), 1, 2).reshape(
        layers, fsdp_size * d_local, col_count
    )
    full_width = columns.shape[1]
    column_blocks = columns.reshape(layers, full_width // BLK, BLK, columns.shape[2])
    left_done = jnp.einsum(
        "lbij,lbjc->lbic", g_all, column_blocks, preferred_element_type=jnp.float32
    )
    left_done = left_done.reshape(columns.shape).astype(jnp.bfloat16)
    back = jnp.swapaxes(left_done.reshape(layers, chips, 2, d_local, col_count), 1, 2).reshape(
        layers, fsdp_size * d_local, col_count
    )
    back = lax.all_to_all(back, "core", split_axis=1, concat_axis=2, tiled=True)
    update = lax.all_to_all(back, CHIP_AXES, split_axis=1, concat_axis=2, tiled=True)
    vocab_total = counts.shape[0] * fsdp_size
    frequency = counts.astype(jnp.float32) * vocab_total / count_total
    emb_update = (emb_grad.astype(jnp.float32) / (frequency + EDAMP)[:, None]).astype(jnp.bfloat16)
    return (update, owner_out, emb_update)


def solution(mesh):
    fine = Mesh(np.asarray(mesh.devices).reshape(8, 8, 2, -1), FSDP + ("tensor",))
    placed = (
        P(None, FSDP, "tensor"),
        P(None, FSDP, "tensor"),
        P(None, FSDP, "tensor"),
        P(FSDP, "tensor"),
        P(FSDP),
        P("tensor", None),
    )
    return jax.shard_map(
        on_device,
        mesh=fine,
        in_specs=placed,
        out_specs=(P(None, FSDP, "tensor"), P("tensor", FSDP, None, None), P(FSDP, "tensor")),
        check_vma=False,
    )
```

```python
import jax
import jax.numpy as jnp
from jax import lax
import numpy as np
from jax.sharding import Mesh, PartitionSpec as P

BLK = 128
FSDP_SIZE = 128
CHIP_AXES = ("y", "z")
FSDP = ("y", "z", "core")
NS_ITERS = 8


DAMP = 0.02
EDAMP = 0.25


def newton_inverse(factor):
    identity = jnp.eye(factor.shape[-1], dtype=jnp.float32)
    damped = factor + DAMP * identity
    norm_scale = jnp.max(jnp.sum(jnp.abs(damped), axis=-1), axis=-1)
    approx = identity[None] / norm_scale[:, None, None]

    def sweep(sweep_idx, approx):
        product = jnp.einsum("bij,bjk->bik", damped, approx, precision=lax.Precision.HIGH)
        return jnp.einsum(
            "bij,bjk->bik", approx, 2.0 * identity[None] - product, precision=lax.Precision.HIGH
        )

    return lax.fori_loop(0, NS_ITERS, sweep, approx)


def pack_half(blocks, count_part, rows_out):
    half = BLK // 2
    rows = lax.broadcasted_iota(jnp.int32, (half, BLK), 0)
    lanes = lax.broadcasted_iota(jnp.int32, (half, BLK), 1)
    bottom = blocks[:, half:, :]
    panel = jnp.where(lanes >= rows, blocks[:, :half, :], jnp.roll(bottom, half, axis=2))
    diag = jnp.sum(jnp.where(lanes == rows + half, bottom, 0.0), axis=2).reshape(-1)
    diag_rows = -(-diag.shape[0] // BLK)
    diag = jnp.concatenate([diag, jnp.zeros((diag_rows * BLK - diag.shape[0],), jnp.float32)])
    count_row = jnp.zeros((1, BLK), jnp.float32).at[0, 0].set(count_part)
    body = jnp.concatenate([panel.reshape(-1, BLK), diag.reshape(diag_rows, BLK), count_row], axis=0)
    return jnp.concatenate([body, jnp.zeros((rows_out - body.shape[0], BLK), jnp.float32)], axis=0)


def pack_symmetric(blocks, count_part, fsdp_size):
    share = blocks.shape[0] // 2
    need = share * BLK // 2 + -(-share * BLK // 2 // BLK) + 1
    rows_out = -(-need // (fsdp_size // 2)) * (fsdp_size // 2)
    return jnp.concatenate(
        [pack_half(blocks[:share], count_part, rows_out), pack_half(blocks[share:], count_part, rows_out)]
    )


def unpack_symmetric(summed, block_total):
    half = BLK // 2
    panel = summed[: block_total * half].reshape(block_total, half, BLK)
    diag_rows = -(-block_total * half // BLK)
    diag = summed[block_total * half : block_total * half + diag_rows].reshape(-1)
    diag = diag[: block_total * half].reshape(block_total, half)
    count_total = summed[block_total * half + diag_rows, 0]
    rows = lax.broadcasted_iota(jnp.int32, (half, BLK), 0)
    lanes = lax.broadcasted_iota(jnp.int32, (half, BLK), 1)
    top = jnp.where(lanes >= rows, panel, 0.0)
    turned = jnp.roll(panel, half, axis=2)
    bottom = jnp.where((lanes >= half) & (lanes - half < rows), turned, 0.0)
    bottom = jnp.where(lanes - half == rows, diag[:, :, None], bottom)
    tri = jnp.concatenate([top, bottom], axis=1)
    eye = lax.broadcasted_iota(jnp.int32, (BLK, BLK), 0) == lax.broadcasted_iota(jnp.int32, (BLK, BLK), 1)
    return jnp.where(eye, tri, tri + jnp.swapaxes(tri, 1, 2)), count_total


def sum_over_fsdp(packed, fsdp_size):
    core = lax.axis_index("core")
    chips = fsdp_size // 2
    halves = packed.reshape(2, packed.shape[0] // 2, BLK)
    send = jnp.where(core == 0, halves[1], halves[0])
    keep = jnp.where(core == 0, halves[0], halves[1])
    part = keep + lax.ppermute(send, "core", [(0, 1), (1, 0)])
    chunk = part.shape[0] // chips
    pieces = lax.all_to_all(part.reshape(chips, chunk, BLK), CHIP_AXES, 0, 0, tiled=True)
    mine = jnp.sum(pieces, axis=0)
    spread = jnp.broadcast_to(mine[None], (chips, chunk, BLK))
    return lax.all_to_all(spread, CHIP_AXES, 0, 0, tiled=True).reshape(part.shape)


def on_device(layer_inputs, out_grads, weight_grad, emb_grad, counts, owner_pos):
    fsdp_size = FSDP_SIZE
    layers, row_count, inner_local = layer_inputs.shape
    width_local = out_grads.shape[2]
    a_count = inner_local // BLK
    g_count = width_local // BLK
    input_blocks = layer_inputs.reshape(layers, row_count, a_count, BLK)
    a_part = jnp.einsum(
        "lrbi,lrbj->lbij", input_blocks, input_blocks, preferred_element_type=jnp.float32
    )
    grad_blocks = out_grads.reshape(layers, row_count, g_count, BLK)
    g_part = jnp.einsum(
        "lrbi,lrbj->lbij", grad_blocks, grad_blocks, preferred_element_type=jnp.float32
    )
    block_total = layers * (a_count + g_count)
    partials = jnp.concatenate([a_part, g_part], axis=1).reshape(block_total, BLK, BLK)
    count_part = jnp.sum(counts.astype(jnp.float32))
    packed = pack_symmetric(partials, count_part, fsdp_size)
    summed = sum_over_fsdp(packed, fsdp_size)
    share = block_total // 2
    blocks_sum, count_total = unpack_symmetric(summed, share)
    divisor = row_count * fsdp_size
    core = lax.axis_index(FSDP) % 2
    mine = newton_inverse(blocks_sum / divisor)
    other = lax.ppermute(mine, FSDP, [(i, i ^ 1) for i in range(fsdp_size)])
    inv = jnp.where(core == 0, jnp.concatenate([mine, other]), jnp.concatenate([other, mine]))
    own_table = owner_pos[0]
    slot = lax.axis_index(FSDP)
    hit = own_table == slot
    pick = jnp.argmax(hit)
    held = lax.dynamic_index_in_dim(inv, pick, axis=0, keepdims=True)
    owner_out = jnp.where(jnp.any(hit), held, 0.0)[None]
    low_inv = inv.astype(jnp.bfloat16).reshape(layers, a_count + g_count, BLK, BLK)
    a_low = low_inv[:, :a_count]
    g_own = low_inv[:, a_count:]
    g_all = lax.all_gather(g_own, "tensor", axis=1, tiled=True)
    d_local = weight_grad.shape[1]
    grad_split = weight_grad.reshape(layers, d_local, a_count, BLK)
    right_done = jnp.einsum(
        "ldbi,lbij->ldbj", grad_split, a_low, preferred_element_type=jnp.float32
    )
    right_done = right_done.reshape(layers, d_local, inner_local).astype(jnp.bfloat16)
    columns = lax.all_to_all(right_done, FSDP, split_axis=2, concat_axis=1, tiled=True)
    full_width = columns.shape[1]
    column_blocks = columns.reshape(layers, full_width // BLK, BLK, columns.shape[2])
    left_done = jnp.einsum(
        "lbij,lbjc->lbic", g_all, column_blocks, preferred_element_type=jnp.float32
    )
    left_done = left_done.reshape(columns.shape).astype(jnp.bfloat16)
    update = lax.all_to_all(left_done, FSDP, split_axis=1, concat_axis=2, tiled=True)
    vocab_total = counts.shape[0] * fsdp_size
    frequency = counts.astype(jnp.float32) * vocab_total / count_total
    emb_update = (emb_grad.astype(jnp.float32) / (frequency + EDAMP)[:, None]).astype(jnp.bfloat16)
    return (update, owner_out, emb_update)


def solution(mesh):
    fine = Mesh(np.asarray(mesh.devices).reshape(8, 8, 2, -1), FSDP + ("tensor",))
    placed = (
        P(None, FSDP, "tensor"),
        P(None, FSDP, "tensor"),
        P(None, FSDP, "tensor"),
        P(FSDP, "tensor"),
        P(FSDP),
        P("tensor", None),
    )
    return jax.shard_map(
        on_device,
        mesh=fine,
        in_specs=placed,
        out_specs=(P(None, FSDP, "tensor"), P("tensor", FSDP, None, None), P(FSDP, "tensor")),
        check_vma=False,
    )
```
